32 devices in a mesh: grp: 2 (over y), srv: 16 (over z, x, core).
Axes of the slice: x: 2, y: 2, z: 4, core: 2. Of those that a mesh axis runs over, the one named last changes fastest.
Arguments:
- queries: bfloat16 [12288, 1536], P(('grp', 'srv')), parts along dimension 0, may hold values from -4096 to 4096
- latent_rope: bfloat16 [12288, 576], P(('grp', 'srv')), parts along dimension 0, may hold values from -16 to 16
- doc_start: int32 [12288], P(('grp', 'srv')), parts along dimension 0, may hold values from 0 to 6143, as said below
- w_kv_up: bfloat16 [512, 2048], replicated, may hold values from -0.25 to 0.25
- w_out: bfloat16 [1024, 2048], replicated, may hold values from -0.5 to 0.5
Outputs:
- mixed: bfloat16 [12288, 2048], P(('grp', 'srv')), parts along dimension 0
The draws below stay inside these ranges and needn't reach their ends.
There are 2 independent parts, one for each index of `grp`. The reference program is written for one: setup_inputs(seed, part) draws one part's arguments, and reference() takes and returns one part's arrays. A program takes and returns all parts, laid end to end along the dimension named above; an argument that names none is the same for every part. Nothing has to cross between parts.
Inputs may be any that keep to these rules, and one draw needn't show every extreme that they name: doc_start[i] <= i < doc_start[i] + 2688; doc_start[i] is i or doc_start[i-1]; the first document has exactly 2688 positions.
All inputs are finite; a program needn't handle non-finite values.
Results may differ from the reference program's by a relative error of at most 0.0063.
Values may be sent and summed in bfloat16 or wider, within the bound.
No kernel may reach another device: no remote copies, remote signals or barrier semaphores. Data moves between devices by JAX's collectives and lax.ppermute only.
A program may use at most 128 MiB of HBM per device.

```python
import math
import jax
import jax.numpy as jnp
from jax import lax

D = 2048
H = 8
DN = 128
DR = 64
DV = 128
R = 512
TOK_DEV = 384
REACH = 7
TOKENS = 6144
DOCMAX = 2688


def draw_common(key):
    latent = jax.random.normal(jax.random.fold_in(key, 101), (TOKENS, R + DR), jnp.float32)
    query_all = jax.random.normal(jax.random.fold_in(key, 202), (TOKENS, H, DN + DR), jnp.float32)
    return (latent, query_all)


def draw_queries(key, part):
    latent, query_all = draw_common(key)
    return query_all.reshape(TOKENS, H * (DN + DR)).astype(jnp.bfloat16)


def draw_latent_rope(key, part):
    latent, query_all = draw_common(key)
    return latent.astype(jnp.bfloat16)


def draw_doc_start(key, part):
    lengths = jax.random.randint(jax.random.fold_in(key, 404), (TOKENS,), 1, DOCMAX + 1).astype(jnp.int32)
    lengths = lengths.at[0].set(DOCMAX)
    starts = (jnp.cumsum(lengths) - lengths).astype(jnp.int32)
    positions = jnp.arange(TOKENS, dtype=jnp.int32)
    doc_index = (jnp.searchsorted(starts, positions, side='right') - 1).astype(jnp.int32)
    return starts[doc_index].astype(jnp.int32)


def centred(rng, dims, width, bound, kind=jnp.bfloat16):
    values = width * jax.random.normal(rng, dims, jnp.float32)
    return jnp.clip(values, min=-bound, max=bound).astype(kind)


def setup_inputs(seed: int = 0, part: int = 0) -> dict:
    keys = jax.random.split(jax.random.key(seed), 6)
    own_keys = jax.random.split(jax.random.fold_in(keys[5], part), 6)
    return {
        "queries": draw_queries(jax.random.fold_in(jax.random.fold_in(keys[5], part), 71), part),
        "latent_rope": draw_latent_rope(jax.random.fold_in(jax.random.fold_in(keys[5], part), 71), part),
        "doc_start": draw_doc_start(jax.random.fold_in(jax.random.fold_in(keys[5], part), 71), part),
        "w_kv_up": centred(keys[3], (R, H * (DN + DV)), R ** -0.5, 0.25),
        "w_out": centred(keys[4], (H * DV, D), DV ** -0.5, 0.5),
    }


def block_terms(query_nope, query_rope, key_nope, values, key_rope, query_pos, key_pos, starts):
    score_scale = 1.0 / math.sqrt(DN + DR)
    scores = jnp.einsum('ihc,jhc->hij', query_nope.astype(jnp.float32), key_nope.astype(jnp.float32))
    scores = scores + jnp.einsum('ihc,jc->hij', query_rope.astype(jnp.float32), key_rope.astype(jnp.float32))
    scores = scores * score_scale
    allowed = (key_pos[None, :] >= starts[:, None]) & (key_pos[None, :] <= query_pos[:, None])
    masked = jnp.where(allowed[None], scores, -jnp.inf)
    block_max = jnp.maximum(lax.optimization_barrier(jnp.max(masked, axis=2)), jnp.float32(-1e+30))
    weights = jnp.where(allowed[None], jnp.exp(scores - block_max[:, :, None]), jnp.float32(0.0))
    block_total = lax.optimization_barrier(jnp.sum(weights, axis=2))
    rounded = lax.optimization_barrier(weights.astype(jnp.bfloat16))
    block_out = jnp.einsum('hij,jhc->ihc', rounded.astype(jnp.float32), values.astype(jnp.float32))
    return (block_out, block_max, block_total)

def merge_blocks(pieces):
    top_max = pieces[0][1]
    for block_part in pieces[1:]:
        top_max = jnp.maximum(top_max, block_part[1])
    numerator = jnp.zeros(pieces[0][0].shape, jnp.float32)
    denominator = jnp.zeros(pieces[0][0].shape[:2] + (1,), jnp.float32)
    for block_part in pieces:
        factor = jnp.exp(block_part[1] - top_max)
        numerator = numerator + factor.T[:, :, None] * block_part[0]
        denominator = denominator + (factor * block_part[2]).T[:, :, None]
    return (numerator / denominator).astype(jnp.bfloat16)

def reference(queries, latent_rope, doc_start, w_kv_up, w_out):
    blocks = TOKENS // TOK_DEV
    keys_values = jnp.dot(latent_rope[:, :R], w_kv_up, preferred_element_type=jnp.float32).astype(jnp.bfloat16)
    keys_values = keys_values.reshape(blocks, TOK_DEV, H, DN + DV)
    key_ropes = latent_rope[:, R:].reshape(blocks, TOK_DEV, DR)
    query_blocks = queries.reshape(blocks, TOK_DEV, H, DN + DR)
    start_blocks = doc_start.reshape(blocks, TOK_DEV)
    offsets = jnp.arange(TOK_DEV, dtype=jnp.int32)

    def attend_block(block_index):
        query_here = query_blocks[block_index]
        starts = start_blocks[block_index]
        query_pos = block_index * TOK_DEV + offsets
        pieces = []
        for distance in range(REACH + 1):
            source = jnp.maximum(block_index - distance, 0).astype(jnp.int32)
            key_kv = keys_values[source]
            key_pos = query_pos - distance * TOK_DEV
            pieces.append(block_terms(query_here[:, :, :DN], query_here[:, :, DN:], key_kv[:, :, :DN], key_kv[:, :, DN:], key_ropes[source], query_pos, key_pos, starts))
        return merge_blocks(pieces)
    attended = lax.map(attend_block, jnp.arange(blocks, dtype=jnp.int32))
    attended = attended.reshape(TOKENS, H * DV)
    return jnp.dot(attended, w_out, preferred_element_type=jnp.float32).astype(jnp.bfloat16)
```

```python
import math

import jax
import jax.numpy as jnp
from jax import lax
from jax.sharding import PartitionSpec as P

DN = 128
DR = 64
DV = 128
R = 512
REACH = 7


def passed_along(value, axis, steps):
    count = lax.axis_size(axis)
    initial, last = (max(0, -steps), min(count, count - steps))
    return lax.ppermute(value, axis, [(source, source + steps) for source in range(initial, last)])


def expand_rows(latent_part, w_kv_up, head_count):
    row_count = latent_part.shape[0]
    product = jnp.dot(latent_part, w_kv_up, preferred_element_type=jnp.float32)
    return product.astype(jnp.bfloat16).reshape(row_count, head_count, -1)


def block_terms(query_nope, query_rope, key_nope, values, key_rope, query_pos, key_pos, starts):
    score_scale = 1.0 / math.sqrt(query_nope.shape[-1] + query_rope.shape[-1])
    scores = jnp.einsum("ihc,jhc->hij", query_nope, key_nope, preferred_element_type=jnp.float32)
    scores = scores + jnp.einsum(
        "ihc,jc->hij", query_rope, key_rope, preferred_element_type=jnp.float32
    )
    scores = scores * score_scale
    allowed = (key_pos[None, :] >= starts[:, None]) & (key_pos[None, :] <= query_pos[:, None])
    masked = jnp.where(allowed[None], scores, -jnp.inf)
    block_max = jnp.maximum(jnp.max(masked, axis=2), jnp.float32(-1e30))
    weights = jnp.where(allowed[None], jnp.exp(scores - block_max[:, :, None]), jnp.float32(0.0))
    block_total = jnp.sum(weights, axis=2)
    block_out = jnp.einsum(
        "hij,jhc->ihc", weights.astype(jnp.bfloat16), values, preferred_element_type=jnp.float32
    )
    return (block_out, block_max, block_total)


def merge_blocks(pieces):
    top_max = pieces[0][1]
    for block_part in pieces[1:]:
        top_max = jnp.maximum(top_max, block_part[1])
    numerator = jnp.zeros(pieces[0][0].shape, jnp.float32)
    denominator = jnp.zeros(pieces[0][0].shape[:2] + (1,), jnp.float32)
    for block_part in pieces:
        factor = jnp.exp(block_part[1] - top_max)
        numerator = numerator + factor.T[:, :, None] * block_part[0]
        denominator = denominator + (factor * block_part[2]).T[:, :, None]
    return (numerator / denominator).astype(jnp.bfloat16)


def local(queries, latent_rope, doc_start, w_kv_up, w_out):
    row_count = queries.shape[0]
    head_count = w_out.shape[0] // DV
    query_all = queries.reshape(row_count, head_count, DN + DR)
    query_nope = query_all[:, :, :DN]
    query_rope = query_all[:, :, DN:]
    device_slot = lax.axis_index("srv")
    query_pos = device_slot * row_count + jnp.arange(row_count, dtype=jnp.int32)
    pieces = []
    held = latent_rope
    for distance in range(REACH + 1):
        if distance > 0:
            held = passed_along(held, "srv", 1)
        key_kv = expand_rows(held[:, :R], w_kv_up, head_count)
        key_rope = held[:, R:]
        key_pos = query_pos - distance * row_count
        pieces.append(
            block_terms(
                query_nope,
                query_rope,
                key_kv[:, :, :DN],
                key_kv[:, :, DN:],
                key_rope,
                query_pos,
                key_pos,
                doc_start,
            )
        )
    attended = merge_blocks(pieces).reshape(row_count, head_count * DV)
    return jnp.dot(attended, w_out, preferred_element_type=jnp.float32).astype(jnp.bfloat16)


def solution(mesh):
    in_specs = (P(("grp", "srv"), None), P(("grp", "srv"), None), P(("grp", "srv")), P(), P())
    out_specs = P(("grp", "srv"), None)
    return jax.shard_map(local, mesh=mesh, in_specs=in_specs, out_specs=out_specs, check_vma=False)
```

```python
import math

import jax
import jax.numpy as jnp
from jax import lax
from jax.sharding import PartitionSpec as P

DN = 128
DR = 64
DV = 128
R = 512
REACH = 7


def moved(value, pairs):
    return lax.ppermute(value, "srv", pairs)


def even_distance_blocks(own):
    count = lax.axis_size("srv")
    slots = range(count)
    k_of = lambda s: s % 4
    near = moved(own, [(s, s + 2) for s in slots if k_of(s) < 2])
    back4 = moved(own, [(s, s + 4) for s in slots if s + 4 < count])
    across = moved(back4, [(s, s ^ 2) for s in slots])
    back8 = moved(back4, [(s, s + 4) for s in slots if s + 4 < count and k_of(s) != 0])
    far = moved(back8, [(s, s - 2) for s in slots if k_of(s) >= 2])
    low_half = lax.axis_index("srv") % 4 < 2
    dist2 = jnp.where(low_half, across, near)
    dist6 = jnp.where(low_half, far, across)
    return [own, dist2, back4, dist6, back8]


def odd_distance_block(nearer, farther):
    count = lax.axis_size("srv")
    upper_core = lax.axis_index("srv") % 2 == 1
    sent = jnp.where(upper_core, farther, nearer)
    return moved(sent, [(s, s ^ 1) for s in range(count)])


def expand_rows(latent_part, w_kv_up, head_count):
    row_count = latent_part.shape[0]
    product = jnp.dot(latent_part, w_kv_up, preferred_element_type=jnp.float32)
    return product.astype(jnp.bfloat16).reshape(row_count, head_count, -1)


def block_terms(query_nope, query_rope, key_nope, values, key_rope, query_pos, key_pos, starts):
    score_scale = 1.0 / math.sqrt(query_nope.shape[-1] + query_rope.shape[-1])
    scores = jnp.einsum("ihc,jhc->hij", query_nope, key_nope, preferred_element_type=jnp.float32)
    scores = scores + jnp.einsum(
        "ihc,jc->hij", query_rope, key_rope, preferred_element_type=jnp.float32
    )
    scores = scores * score_scale
    allowed = (key_pos[None, :] >= starts[:, None]) & (key_pos[None, :] <= query_pos[:, None])
    masked = jnp.where(allowed[None], scores, -jnp.inf)
    block_max = jnp.maximum(jnp.max(masked, axis=2), jnp.float32(-1e30))
    weights = jnp.where(allowed[None], jnp.exp(scores - block_max[:, :, None]), jnp.float32(0.0))
    block_total = jnp.sum(weights, axis=2)
    block_out = jnp.einsum(
        "hij,jhc->ihc", weights.astype(jnp.bfloat16), values, preferred_element_type=jnp.float32
    )
    return (block_out, block_max, block_total)


def merge_blocks(pieces):
    top_max = pieces[0][1]
    for block_part in pieces[1:]:
        top_max = jnp.maximum(top_max, block_part[1])
    numerator = jnp.zeros(pieces[0][0].shape, jnp.float32)
    denominator = jnp.zeros(pieces[0][0].shape[:2] + (1,), jnp.float32)
    for block_part in pieces:
        factor = jnp.exp(block_part[1] - top_max)
        numerator = numerator + factor.T[:, :, None] * block_part[0]
        denominator = denominator + (factor * block_part[2]).T[:, :, None]
    return (numerator / denominator).astype(jnp.bfloat16)


def local(queries, latent_rope, doc_start, w_kv_up, w_out):
    row_count = queries.shape[0]
    head_count = w_out.shape[0] // DV
    query_all = queries.reshape(row_count, head_count, DN + DR)
    query_nope = query_all[:, :, :DN]
    query_rope = query_all[:, :, DN:]
    device_slot = lax.axis_index("srv")
    query_pos = device_slot * row_count + jnp.arange(row_count, dtype=jnp.int32)
    evens = even_distance_blocks(latent_rope)
    held_at = {2 * j: evens[j] for j in range(5)}
    for j in range(1, 5):
        held_at[2 * j - 1] = odd_distance_block(evens[j - 1], evens[j])
    pieces = []
    for distance in range(REACH + 1):
        held = held_at[distance]
        key_kv = expand_rows(held[:, :R], w_kv_up, head_count)
        key_rope = held[:, R:]
        key_pos = query_pos - distance * row_count
        pieces.append(
            block_terms(
                query_nope,
                query_rope,
                key_kv[:, :, :DN],
                key_kv[:, :, DN:],
                key_rope,
                query_pos,
                key_pos,
                doc_start,
            )
        )
    attended = merge_blocks(pieces).reshape(row_count, head_count * DV)
    return jnp.dot(attended, w_out, preferred_element_type=jnp.float32).astype(jnp.bfloat16)


def solution(mesh):
    in_specs = (P(("grp", "srv"), None), P(("grp", "srv"), None), P(("grp", "srv")), P(), P())
    out_specs = P(("grp", "srv"), None)
    return jax.shard_map(local, mesh=mesh, in_specs=in_specs, out_specs=out_specs, check_vma=False)
```

```python
import functools
import math

import jax
import jax.numpy as jnp
from jax import lax
from jax.experimental import pallas as pl
from jax.experimental.pallas import tpu as pltpu
from jax.sharding import PartitionSpec as P

DN = 128
DR = 64
DV = 128
R = 512
REACH = 7


def moved(value, pairs):
    return lax.ppermute(value, "srv", pairs)


def even_distance_blocks(own):
    count = lax.axis_size("srv")
    slots = range(count)
    k_of = lambda s: s % 4
    near = moved(own, [(s, s + 2) for s in slots if k_of(s) < 2])
    back4 = moved(own, [(s, s + 4) for s in slots if s + 4 < count])
    across = moved(back4, [(s, s ^ 2) for s in slots])
    back8 = moved(back4, [(s, s + 4) for s in slots if s + 4 < count and k_of(s) != 0])
    far = moved(back8, [(s, s - 2) for s in slots if k_of(s) >= 2])
    low_half = lax.axis_index("srv") % 4 < 2
    dist2 = jnp.where(low_half, across, near)
    dist6 = jnp.where(low_half, far, across)
    return [own, dist2, back4, dist6, back8]


def odd_distance_block(nearer, farther):
    count = lax.axis_size("srv")
    upper_core = lax.axis_index("srv") % 2 == 1
    sent = jnp.where(upper_core, farther, nearer)
    return moved(sent, [(s, s ^ 1) for s in range(count)])


def distance_kernel(flag_ref, qn_ref, qr_ref, lat_ref, w_ref, rel_ref, o_ref, m_ref, l_ref, *, distance):
    rows = lat_ref.shape[0]

    @pl.when(flag_ref[0] == 0)
    def _():
        o_ref[...] = jnp.zeros(o_ref.shape, jnp.float32)
        m_ref[...] = jnp.full(m_ref.shape, -1e30, jnp.float32)
        l_ref[...] = jnp.zeros(l_ref.shape, jnp.float32)

    @pl.when(flag_ref[0] != 0)
    def _():
        score_scale = 1.0 / math.sqrt(DN + DR)
        kv = jnp.dot(lat_ref[:, :R], w_ref[...], preferred_element_type=jnp.float32).astype(jnp.bfloat16)
        key_nope = kv[:, :DN]
        values = kv[:, DN:]
        key_rope = lat_ref[:, R:]
        contract = (((1,), (1,)), ((), ()))
        scores = lax.dot_general(qn_ref[0], key_nope, contract, preferred_element_type=jnp.float32)
        scores = scores + lax.dot_general(qr_ref[0], key_rope, contract, preferred_element_type=jnp.float32)
        scores = scores * score_scale
        col = lax.broadcasted_iota(jnp.int32, (rows, rows), 1)
        allowed = col >= rel_ref[...] + distance * rows
        if distance == 0:
            allowed = allowed & (col <= lax.broadcasted_iota(jnp.int32, (rows, rows), 0))
        masked = jnp.where(allowed, scores, -jnp.inf)
        block_max = jnp.maximum(jnp.max(masked, axis=1, keepdims=True), jnp.float32(-1e30))
        weights = jnp.where(allowed, jnp.exp(scores - block_max), jnp.float32(0.0))
        l_ref[0] = jnp.sum(weights, axis=1, keepdims=True)
        m_ref[0] = block_max
        o_ref[...] = jnp.dot(weights.astype(jnp.bfloat16), values, preferred_element_type=jnp.float32)


def distance_terms(flag, query_nope, query_rope, latent_block, w_kv_up, rel_start, distance):
    head_count, rows, _ = query_nope.shape
    width = latent_block.shape[1]
    flops = head_count * rows * (2 * R * (DN + DV) + 2 * rows * (DN + DR + DV))
    return pl.pallas_call(
        functools.partial(distance_kernel, distance=distance),
        out_shape=(
            jax.ShapeDtypeStruct((rows, head_count * DV), jnp.float32),
            jax.ShapeDtypeStruct((head_count, rows, 1), jnp.float32),
            jax.ShapeDtypeStruct((head_count, rows, 1), jnp.float32),
        ),
        grid_spec=pltpu.PrefetchScalarGridSpec(
            num_scalar_prefetch=1,
            grid=(head_count,),
            in_specs=[
                pl.BlockSpec((1, rows, DN), lambda h, f: (h, 0, 0)),
                pl.BlockSpec((1, rows, DR), lambda h, f: (h, 0, 0)),
                pl.BlockSpec((rows, width), lambda h, f: (0, 0)),
                pl.BlockSpec((R, DN + DV), lambda h, f: (0, h)),
                pl.BlockSpec((rows, 1), lambda h, f: (0, 0)),
            ],
            out_specs=[
                pl.BlockSpec((rows, DV), lambda h, f: (0, h)),
                pl.BlockSpec((1, rows, 1), lambda h, f: (h, 0, 0)),
                pl.BlockSpec((1, rows, 1), lambda h, f: (h, 0, 0)),
            ],
        ),
        compiler_params=pltpu.CompilerParams(dimension_semantics=("arbitrary",)),
        cost_estimate=pl.CostEstimate(
            flops=flops, transcendentals=head_count * rows * rows, bytes_accessed=6 * 1024 * 1024
        ),
    )(flag, query_nope, query_rope, latent_block, w_kv_up, rel_start)


def merge_blocks(pieces):
    top_max = pieces[0][1]
    for block_part in pieces[1:]:
        top_max = jnp.maximum(top_max, block_part[1])
    numerator = jnp.zeros(pieces[0][0].shape, jnp.float32)
    denominator = jnp.zeros(pieces[0][0].shape[:2] + (1,), jnp.float32)
    for block_part in pieces:
        factor = jnp.exp(block_part[1] - top_max)
        numerator = numerator + factor.T[:, :, None] * block_part[0]
        denominator = denominator + (factor * block_part[2]).T[:, :, None]
    return (numerator / denominator).astype(jnp.bfloat16)


def local(queries, latent_rope, doc_start, w_kv_up, w_out):
    row_count = queries.shape[0]
    head_count = w_out.shape[0] // DV
    query_all = queries.reshape(row_count, head_count, DN + DR).transpose(1, 0, 2)
    query_nope = query_all[:, :, :DN]
    query_rope = query_all[:, :, DN:]
    device_slot = lax.axis_index("srv")
    block_first = device_slot * row_count
    rel_start = (doc_start - block_first).reshape(row_count, 1)
    lowest_start = jnp.min(doc_start)
    evens = even_distance_blocks(latent_rope)
    held_at = {2 * j: evens[j] for j in range(5)}
    for j in range(1, 5):
        held_at[2 * j - 1] = odd_distance_block(evens[j - 1], evens[j])
    pieces = []
    for distance in range(REACH + 1):
        key_last = block_first - distance * row_count + row_count - 1
        flag = (key_last >= lowest_start).astype(jnp.int32).reshape(1)
        block_out, block_max, block_total = distance_terms(
            flag, query_nope, query_rope, held_at[distance], w_kv_up, rel_start, distance
        )
        pieces.append((block_out.reshape(row_count, head_count, DV), block_max[:, :, 0], block_total[:, :, 0]))
    attended = merge_blocks(pieces).reshape(row_count, head_count * DV)
    return jnp.dot(attended, w_out, preferred_element_type=jnp.float32).astype(jnp.bfloat16)


def solution(mesh):
    in_specs = (P(("grp", "srv"), None), P(("grp", "srv"), None), P(("grp", "srv")), P(), P())
    out_specs = P(("grp", "srv"), None)
    return jax.shard_map(local, mesh=mesh, in_specs=in_specs, out_specs=out_specs, check_vma=False)
```

```python
import functools
import math

import jax
import jax.numpy as jnp
from jax import lax
from jax.experimental import pallas as pl
from jax.experimental.pallas import tpu as pltpu
from jax.sharding import PartitionSpec as P

DN = 128
DR = 64
DV = 128
R = 512
REACH = 7


def moved(value, pairs):
    return lax.ppermute(value, "srv", pairs)


def even_distance_blocks(own):
    count = lax.axis_size("srv")
    slots = range(count)
    k_of = lambda s: s % 4
    near = moved(own, [(s, s + 2) for s in slots if k_of(s) < 2])
    back4 = moved(own, [(s, s + 4) for s in slots if s + 4 < count])
    across = moved(back4, [(s, s ^ 2) for s in slots])
    back8 = moved(back4, [(s, s + 4) for s in slots if s + 4 < count and k_of(s) != 0])
    far = moved(back8, [(s, s - 2) for s in slots if k_of(s) >= 2])
    low_half = lax.axis_index("srv") % 4 < 2
    dist2 = jnp.where(low_half, across, near)
    dist6 = jnp.where(low_half, far, across)
    return [own, dist2, back4, dist6, back8]


def odd_distance_block(nearer, farther):
    count = lax.axis_size("srv")
    upper_core = lax.axis_index("srv") % 2 == 1
    sent = jnp.where(upper_core, farther, nearer)
    return moved(sent, [(s, s ^ 1) for s in range(count)])


def attend_kernel(flag_ref, qn_ref, qr_ref, w_ref, rel_ref, *rest):
    latent_refs = rest[: REACH + 1]
    out_ref, o_sc, m_sc, l_sc = rest[REACH + 1 :]
    rows = latent_refs[0].shape[0]
    score_scale = 1.0 / math.sqrt(DN + DR)
    contract = (((1,), (1,)), ((), ()))
    col = lax.broadcasted_iota(jnp.int32, (rows, rows), 1)
    row = lax.broadcasted_iota(jnp.int32, (rows, rows), 0)
    rel = rel_ref[...]
    for distance in range(REACH + 1):
        lat_ref = latent_refs[distance]

        @pl.when(flag_ref[distance] == 0)
        def _():
            o_sc[distance] = jnp.zeros((rows, DV), jnp.float32)
            m_sc[distance] = jnp.full((rows, 1), -1e30, jnp.float32)
            l_sc[distance] = jnp.zeros((rows, 1), jnp.float32)

        @pl.when(flag_ref[distance] != 0)
        def _():
            kv = jnp.dot(lat_ref[:, :R], w_ref[...], preferred_element_type=jnp.float32).astype(jnp.bfloat16)
            scores = lax.dot_general(qn_ref[0], kv[:, :DN], contract, preferred_element_type=jnp.float32)
            scores = scores + lax.dot_general(
                qr_ref[0], lat_ref[:, R:], contract, preferred_element_type=jnp.float32
            )
            scores = scores * score_scale
            allowed = col >= rel + distance * rows
            if distance == 0:
                allowed = allowed & (col <= row)
            masked = jnp.where(allowed, scores, -jnp.inf)
            block_max = jnp.maximum(jnp.max(masked, axis=1, keepdims=True), jnp.float32(-1e30))
            weights = jnp.where(allowed, jnp.exp(scores - block_max), jnp.float32(0.0))
            l_sc[distance] = jnp.sum(weights, axis=1, keepdims=True)
            m_sc[distance] = block_max
            o_sc[distance] = jnp.dot(
                weights.astype(jnp.bfloat16), kv[:, DN:], preferred_element_type=jnp.float32
            )

    top_max = m_sc[0]
    for distance in range(1, REACH + 1):
        top_max = jnp.maximum(top_max, m_sc[distance])
    numerator = jnp.zeros((rows, DV), jnp.float32)
    denominator = jnp.zeros((rows, 1), jnp.float32)
    for distance in range(REACH + 1):
        factor = jnp.exp(m_sc[distance] - top_max)
        numerator = numerator + factor * o_sc[distance]
        denominator = denominator + factor * l_sc[distance]
    out_ref[...] = (numerator / denominator).astype(out_ref.dtype)


def attend(flags, query_nope, query_rope, w_kv_up, rel_start, latent_blocks):
    head_count, rows, _ = query_nope.shape
    width = latent_blocks[0].shape[1]
    blocks = len(latent_blocks)
    flops = head_count * blocks * rows * (2 * R * (DN + DV) + 2 * rows * (DN + DR + DV))
    latent_spec = pl.BlockSpec((rows, width), lambda h, f: (0, 0))
    return pl.pallas_call(
        attend_kernel,
        out_shape=jax.ShapeDtypeStruct((rows, head_count * DV), jnp.bfloat16),
        grid_spec=pltpu.PrefetchScalarGridSpec(
            num_scalar_prefetch=1,
            grid=(head_count,),
            in_specs=[
                pl.BlockSpec((1, rows, DN), lambda h, f: (h, 0, 0)),
                pl.BlockSpec((1, rows, DR), lambda h, f: (h, 0, 0)),
                pl.BlockSpec((R, DN + DV), lambda h, f: (0, h)),
                pl.BlockSpec((rows, 1), lambda h, f: (0, 0)),
            ]
            + [latent_spec] * blocks,
            out_specs=pl.BlockSpec((rows, DV), lambda h, f: (0, h)),
            scratch_shapes=[
                pltpu.VMEM((blocks, rows, DV), jnp.float32),
                pltpu.VMEM((blocks, rows, 1), jnp.float32),
                pltpu.VMEM((blocks, rows, 1), jnp.float32),
            ],
        ),
        compiler_params=pltpu.CompilerParams(dimension_semantics=("arbitrary",)),
        cost_estimate=pl.CostEstimate(
            flops=flops, transcendentals=head_count * blocks * rows * rows, bytes_accessed=8 * 1024 * 1024
        ),
    )(flags, query_nope, query_rope, w_kv_up, rel_start, *latent_blocks)


def local(queries, latent_rope, doc_start, w_kv_up, w_out):
    row_count = queries.shape[0]
    head_count = w_out.shape[0] // DV
    query_all = queries.reshape(row_count, head_count, DN + DR).transpose(1, 0, 2)
    query_nope = query_all[:, :, :DN]
    query_rope = query_all[:, :, DN:]
    device_slot = lax.axis_index("srv")
    block_first = device_slot * row_count
    rel_start = (doc_start - block_first).reshape(row_count, 1)
    lowest_start = jnp.min(doc_start)
    evens = even_distance_blocks(latent_rope)
    held_at = {2 * j: evens[j] for j in range(5)}
    for j in range(1, 5):
        held_at[2 * j - 1] = odd_distance_block(evens[j - 1], evens[j])
    distances = jnp.arange(REACH + 1, dtype=jnp.int32)
    key_last = block_first - distances * row_count + row_count - 1
    flags = (key_last >= lowest_start).astype(jnp.int32)
    attended = attend(
        flags, query_nope, query_rope, w_kv_up, rel_start, [held_at[d] for d in range(REACH + 1)]
    )
    return jnp.dot(attended, w_out, preferred_element_type=jnp.float32).astype(jnp.bfloat16)


def solution(mesh):
    in_specs = (P(("grp", "srv"), None), P(("grp", "srv"), None), P(("grp", "srv")), P(), P())
    out_specs = P(("grp", "srv"), None)
    return jax.shard_map(local, mesh=mesh, in_specs=in_specs, out_specs=out_specs, check_vma=False)
```

```python
import functools
import math

import jax
import jax.numpy as jnp
from jax import lax
from jax.experimental import pallas as pl
from jax.experimental.pallas import tpu as pltpu
from jax.sharding import PartitionSpec as P

DN = 128
DR = 64
DV = 128
R = 512
REACH = 7


def moved(value, pairs):
    return lax.ppermute(value, "srv", pairs)


def even_distance_blocks(own):
    count = lax.axis_size("srv")
    slots = range(count)
    k_of = lambda s: s % 4
    near = moved(own, [(s, s + 2) for s in slots if k_of(s) < 2])
    back4 = moved(own, [(s, s + 4) for s in slots if s + 4 < count])
    across = moved(back4, [(s, s ^ 2) for s in slots])
    back8 = moved(back4, [(s, s + 4) for s in slots if s + 4 < count and k_of(s) != 0])
    far = moved(back8, [(s, s - 2) for s in slots if k_of(s) >= 2])
    low_half = lax.axis_index("srv") % 4 < 2
    dist2 = jnp.where(low_half, across, near)
    dist6 = jnp.where(low_half, far, across)
    return [own, dist2, back4, dist6, back8]


def odd_distance_block(nearer, farther):
    count = lax.axis_size("srv")
    upper_core = lax.axis_index("srv") % 2 == 1
    sent = jnp.where(upper_core, farther, nearer)
    return moved(sent, [(s, s ^ 1) for s in range(count)])


def attend_kernel(flag_ref, qn_ref, qr_ref, rel_ref, *rest):
    latent_refs = rest[: REACH + 1]
    kv_refs = rest[REACH + 1 : 2 * (REACH + 1)]
    out_ref, o_sc, m_sc, l_sc, bias_sc = rest[2 * (REACH + 1) :]
    rows = latent_refs[0].shape[0]
    score_scale = 1.0 / math.sqrt(DN + DR)
    contract = (((1,), (1,)), ((), ()))

    @pl.when(pl.program_id(0) == 0)
    def _():
        col = lax.broadcasted_iota(jnp.int32, (rows, rows), 1)
        rel = rel_ref[...]
        for distance in range(REACH + 1):
            allowed = col >= rel + distance * rows
            if distance == 0:
                allowed = allowed & (col <= lax.broadcasted_iota(jnp.int32, (rows, rows), 0))
            bias_sc[distance] = jnp.where(allowed, jnp.float32(0.0), -jnp.inf)

    for distance in range(REACH + 1):
        lat_ref = latent_refs[distance]
        kv_ref = kv_refs[distance]

        @pl.when(flag_ref[distance] == 0)
        def _():
            o_sc[distance] = jnp.zeros((rows, DV), jnp.float32)
            m_sc[distance] = jnp.full((rows, 1), -1e30, jnp.float32)
            l_sc[distance] = jnp.zeros((rows, 1), jnp.float32)

        @pl.when(flag_ref[distance] != 0)
        def _():
            scores = lax.dot_general(qn_ref[0], kv_ref[:, :DN], contract, preferred_element_type=jnp.float32)
            scores = scores + lax.dot_general(
                qr_ref[0], lat_ref[:, R:], contract, preferred_element_type=jnp.float32
            )
            masked = scores * score_scale + bias_sc[distance]
            block_max = jnp.maximum(jnp.max(masked, axis=1, keepdims=True), jnp.float32(-1e30))
            weights = jnp.exp(masked - block_max)
            l_sc[distance] = jnp.sum(weights, axis=1, keepdims=True)
            m_sc[distance] = block_max
            o_sc[distance] = jnp.dot(
                weights.astype(jnp.bfloat16), kv_ref[:, DN:], preferred_element_type=jnp.float32
            )

    top_max = m_sc[0]
    for distance in range(1, REACH + 1):
        top_max = jnp.maximum(top_max, m_sc[distance])
    numerator = jnp.zeros((rows, DV), jnp.float32)
    denominator = jnp.zeros((rows, 1), jnp.float32)
    for distance in range(REACH + 1):
        factor = jnp.exp(m_sc[distance] - top_max)
        numerator = numerator + factor * o_sc[distance]
        denominator = denominator + factor * l_sc[distance]
    out_ref[...] = (numerator / denominator).astype(out_ref.dtype)


def attend(flags, query_nope, query_rope, rel_start, latent_blocks, kv_blocks):
    head_count, rows, _ = query_nope.shape
    width = latent_blocks[0].shape[1]
    blocks = len(latent_blocks)
    flops = head_count * blocks * rows * 2 * rows * (DN + DR + DV)
    latent_spec = pl.BlockSpec((rows, width), lambda h, f: (0, 0))
    kv_spec = pl.BlockSpec((rows, DN + DV), lambda h, f: (0, h))
    return pl.pallas_call(
        attend_kernel,
        out_shape=jax.ShapeDtypeStruct((rows, head_count * DV), jnp.bfloat16),
        grid_spec=pltpu.PrefetchScalarGridSpec(
            num_scalar_prefetch=1,
            grid=(head_count,),
            in_specs=[
                pl.BlockSpec((1, rows, DN), lambda h, f: (h, 0, 0)),
                pl.BlockSpec((1, rows, DR), lambda h, f: (h, 0, 0)),
                pl.BlockSpec((rows, 1), lambda h, f: (0, 0)),
            ]
            + [latent_spec] * blocks
            + [kv_spec] * blocks,
            out_specs=pl.BlockSpec((rows, DV), lambda h, f: (0, h)),
            scratch_shapes=[
                pltpu.VMEM((blocks, rows, DV), jnp.float32),
                pltpu.VMEM((blocks, rows, 1), jnp.float32),
                pltpu.VMEM((blocks, rows, 1), jnp.float32),
                pltpu.VMEM((blocks, rows, rows), jnp.float32),
            ],
        ),
        compiler_params=pltpu.CompilerParams(dimension_semantics=("arbitrary",)),
        cost_estimate=pl.CostEstimate(
            flops=flops, transcendentals=head_count * blocks * rows * rows, bytes_accessed=16 * 1024 * 1024
        ),
    )(flags, query_nope, query_rope, rel_start, *latent_blocks, *kv_blocks)


def local(queries, latent_rope, doc_start, w_kv_up, w_out):
    row_count = queries.shape[0]
    head_count = w_out.shape[0] // DV
    query_all = queries.reshape(row_count, head_count, DN + DR).transpose(1, 0, 2)
    query_nope = query_all[:, :, :DN]
    query_rope = query_all[:, :, DN:]
    device_slot = lax.axis_index("srv")
    block_first = device_slot * row_count
    rel_start = (doc_start - block_first).reshape(row_count, 1)
    lowest_start = jnp.min(doc_start)
    evens = even_distance_blocks(latent_rope)
    held_at = {2 * j: evens[j] for j in range(5)}
    for j in range(1, 5):
        held_at[2 * j - 1] = odd_distance_block(evens[j - 1], evens[j])
    distances = jnp.arange(REACH + 1, dtype=jnp.int32)
    key_last = block_first - distances * row_count + row_count - 1
    flags = (key_last >= lowest_start).astype(jnp.int32)
    latent_blocks = [held_at[d] for d in range(REACH + 1)]
    kv_blocks = [
        jnp.dot(block[:, :R], w_kv_up, preferred_element_type=jnp.float32).astype(jnp.bfloat16)
        for block in latent_blocks
    ]
    attended = attend(flags, query_nope, query_rope, rel_start, latent_blocks, kv_blocks)
    return jnp.dot(attended, w_out, preferred_element_type=jnp.float32).astype(jnp.bfloat16)


def solution(mesh):
    in_specs = (P(("grp", "srv"), None), P(("grp", "srv"), None), P(("grp", "srv")), P(), P())
    out_specs = P(("grp", "srv"), None)
    return jax.shard_map(local, mesh=mesh, in_specs=in_specs, out_specs=out_specs, check_vma=False)
```

```python
import functools
import math

import jax
import jax.numpy as jnp
from jax import lax
from jax.experimental import pallas as pl
from jax.experimental.pallas import tpu as pltpu
from jax.sharding import PartitionSpec as P

DN = 128
DR = 64
DV = 128
R = 512
REACH = 7


def moved(value, pairs):
    return lax.ppermute(value, "srv", pairs)


def even_distance_blocks(own):
    count = lax.axis_size("srv")
    slots = range(count)
    k_of = lambda s: s % 4
    near = moved(own, [(s, s + 2) for s in slots if k_of(s) < 2])
    back4 = moved(own, [(s, s + 4) for s in slots if s + 4 < count])
    across = moved(back4, [(s, s ^ 2) for s in slots])
    back8 = moved(back4, [(s, s + 4) for s in slots if s + 4 < count and k_of(s) != 0])
    far = moved(back8, [(s, s - 2) for s in slots if k_of(s) >= 2])
    low_half = lax.axis_index("srv") % 4 < 2
    dist2 = jnp.where(low_half, across, near)
    dist6 = jnp.where(low_half, far, across)
    return [own, dist2, back4, dist6, back8]


def odd_distance_block(nearer, farther):
    count = lax.axis_size("srv")
    upper_core = lax.axis_index("srv") % 2 == 1
    sent = jnp.where(upper_core, farther, nearer)
    return moved(sent, [(s, s ^ 1) for s in range(count)])


def attend_kernel(flag_ref, qn_ref, qr_ref, rel_ref, *rest):
    blocks = REACH + 1
    rope_refs = rest[:blocks]
    key_refs = rest[blocks : 2 * blocks]
    value_refs = rest[2 * blocks : 3 * blocks]
    out_ref, o_sc, m_sc, l_sc, bias_sc = rest[3 * blocks :]
    rows = value_refs[0].shape[0]
    score_scale = 1.0 / math.sqrt(DN + DR)

    @pl.when(pl.program_id(0) == 0)
    def _():
        col = lax.broadcasted_iota(jnp.int32, (rows, rows), 1)
        rel = rel_ref[...]
        for distance in range(REACH + 1):
            allowed = col >= rel + distance * rows
            if distance == 0:
                allowed = allowed & (col <= lax.broadcasted_iota(jnp.int32, (rows, rows), 0))
            bias_sc[distance] = jnp.where(allowed, jnp.float32(0.0), -jnp.inf)

    for distance in range(REACH + 1):
        rope_ref = rope_refs[distance]
        key_ref = key_refs[distance]
        value_ref = value_refs[distance]

        @pl.when(flag_ref[distance] == 0)
        def _():
            o_sc[distance] = jnp.zeros((rows, DV), jnp.float32)
            m_sc[distance] = jnp.full((rows, 1), -1e30, jnp.float32)
            l_sc[distance] = jnp.zeros((rows, 1), jnp.float32)

        @pl.when(flag_ref[distance] != 0)
        def _():
            scores = jnp.dot(qn_ref[0], key_ref[...], preferred_element_type=jnp.float32)
            scores = scores + jnp.dot(qr_ref[0], rope_ref[...], preferred_element_type=jnp.float32)
            masked = scores * score_scale + bias_sc[distance]
            block_max = jnp.maximum(jnp.max(masked, axis=1, keepdims=True), jnp.float32(-1e30))
            weights = jnp.exp(masked - block_max)
            l_sc[distance] = jnp.sum(weights, axis=1, keepdims=True)
            m_sc[distance] = block_max
            o_sc[distance] = jnp.dot(
                weights.astype(jnp.bfloat16), value_ref[...], preferred_element_type=jnp.float32
            )

    top_max = m_sc[0]
    for distance in range(1, REACH + 1):
        top_max = jnp.maximum(top_max, m_sc[distance])
    numerator = jnp.zeros((rows, DV), jnp.float32)
    denominator = jnp.zeros((rows, 1), jnp.float32)
    for distance in range(REACH + 1):
        factor = jnp.exp(m_sc[distance] - top_max)
        numerator = numerator + factor * o_sc[distance]
        denominator = denominator + factor * l_sc[distance]
    out_ref[...] = (numerator / denominator).astype(out_ref.dtype)


def attend(flags, query_nope, query_rope, rel_start, rope_blocks, key_blocks, value_blocks):
    head_count, rows, _ = query_nope.shape
    blocks = len(rope_blocks)
    flops = head_count * blocks * rows * 2 * rows * (DN + DR + DV)
    rope_spec = pl.BlockSpec((DR, rows), lambda h, f: (0, 0))
    key_spec = pl.BlockSpec((DN, rows), lambda h, f: (h, 0))
    value_spec = pl.BlockSpec((rows, DV), lambda h, f: (0, h))
    return pl.pallas_call(
        attend_kernel,
        out_shape=jax.ShapeDtypeStruct((rows, head_count * DV), jnp.bfloat16),
        grid_spec=pltpu.PrefetchScalarGridSpec(
            num_scalar_prefetch=1,
            grid=(head_count,),
            in_specs=[
                pl.BlockSpec((1, rows, DN), lambda h, f: (h, 0, 0)),
                pl.BlockSpec((1, rows, DR), lambda h, f: (h, 0, 0)),
                pl.BlockSpec((rows, 1), lambda h, f: (0, 0)),
            ]
            + [rope_spec] * blocks
            + [key_spec] * blocks
            + [value_spec] * blocks,
            out_specs=pl.BlockSpec((rows, DV), lambda h, f: (0, h)),
            scratch_shapes=[
                pltpu.VMEM((blocks, rows, DV), jnp.float32),
                pltpu.VMEM((blocks, rows, 1), jnp.float32),
                pltpu.VMEM((blocks, rows, 1), jnp.float32),
                pltpu.VMEM((blocks, rows, rows), jnp.float32),
            ],
        ),
        compiler_params=pltpu.CompilerParams(dimension_semantics=("arbitrary",)),
        cost_estimate=pl.CostEstimate(
            flops=flops, transcendentals=head_count * blocks * rows * rows, bytes_accessed=16 * 1024 * 1024
        ),
    )(flags, query_nope, query_rope, rel_start, *rope_blocks, *key_blocks, *value_blocks)


def local(queries, latent_rope, doc_start, w_kv_up, w_out):
    row_count = queries.shape[0]
    head_count = w_out.shape[0] // DV
    query_all = queries.reshape(row_count, head_count, DN + DR).transpose(1, 0, 2)
    query_nope = query_all[:, :, :DN]
    query_rope = query_all[:, :, DN:]
    device_slot = lax.axis_index("srv")
    block_first = device_slot * row_count
    rel_start = (doc_start - block_first).reshape(row_count, 1)
    lowest_start = jnp.min(doc_start)
    evens = even_distance_blocks(latent_rope)
    held_at = {2 * j: evens[j] for j in range(5)}
    for j in range(1, 5):
        held_at[2 * j - 1] = odd_distance_block(evens[j - 1], evens[j])
    distances = jnp.arange(REACH + 1, dtype=jnp.int32)
    key_last = block_first - distances * row_count + row_count - 1
    flags = (key_last >= lowest_start).astype(jnp.int32)
    latent_blocks = [held_at[d] for d in range(REACH + 1)]
    w_split = w_kv_up.reshape(R, head_count, 2, DN)
    w_key = w_split[:, :, 0, :].reshape(R, head_count * DN)
    w_value = w_split[:, :, 1, :].reshape(R, head_count * DV)
    key_blocks = [
        jnp.einsum("jr,rc->cj", block[:, :R], w_key, preferred_element_type=jnp.float32).astype(jnp.bfloat16)
        for block in latent_blocks
    ]
    value_blocks = [
        jnp.dot(block[:, :R], w_value, preferred_element_type=jnp.float32).astype(jnp.bfloat16)
        for block in latent_blocks
    ]
    rope_blocks = [block[:, R:].T for block in latent_blocks]
    attended = attend(flags, query_nope, query_rope, rel_start, rope_blocks, key_blocks, value_blocks)
    return jnp.dot(attended, w_out, preferred_element_type=jnp.float32).astype(jnp.bfloat16)


def solution(mesh):
    in_specs = (P(("grp", "srv"), None), P(("grp", "srv"), None), P(("grp", "srv")), P(), P())
    out_specs = P(("grp", "srv"), None)
    return jax.shard_map(local, mesh=mesh, in_specs=in_specs, out_specs=out_specs, check_vma=False)
```

```python
import functools
import math

import jax
import jax.numpy as jnp
from jax import lax
from jax.experimental import pallas as pl
from jax.experimental.pallas import tpu as pltpu
from jax.sharding import PartitionSpec as P

DN = 128
DR = 64
DV = 128
R = 512
REACH = 7


def moved(value, pairs):
    return lax.ppermute(value, "srv", pairs)


def even_distance_blocks(own):
    count = lax.axis_size("srv")
    slots = range(count)
    k_of = lambda s: s % 4
    near = moved(own, [(s, s + 2) for s in slots if k_of(s) < 2])
    back4 = moved(own, [(s, s + 4) for s in slots if s + 4 < count])
    across = moved(back4, [(s, s ^ 2) for s in slots])
    back8 = moved(back4, [(s, s + 4) for s in slots if s + 4 < count and k_of(s) != 0])
    far = moved(back8, [(s, s - 2) for s in slots if k_of(s) >= 2])
    low_half = lax.axis_index("srv") % 4 < 2
    dist2 = jnp.where(low_half, across, near)
    dist6 = jnp.where(low_half, far, across)
    return [own, dist2, back4, dist6, back8]


def odd_distance_block(nearer, farther):
    count = lax.axis_size("srv")
    upper_core = lax.axis_index("srv") % 2 == 1
    sent = jnp.where(upper_core, farther, nearer)
    return moved(sent, [(s, s ^ 1) for s in range(count)])


def attend_kernel(flag_ref, qn_ref, qr_ref, rel_ref, *rest):
    blocks = REACH + 1
    rope_refs = rest[:blocks]
    key_refs = rest[blocks : 2 * blocks]
    value_refs = rest[2 * blocks : 3 * blocks]
    out_ref, o_sc, m_sc, l_sc, bias_sc = rest[3 * blocks :]
    rows = value_refs[0].shape[0]
    score_scale = 1.0 / math.sqrt(DN + DR)

    @pl.when(pl.program_id(0) == 0)
    def _():
        col = lax.broadcasted_iota(jnp.int32, (rows, rows), 1)
        rel = rel_ref[...]
        for distance in range(REACH + 1):
            allowed = col >= rel + distance * rows
            if distance == 0:
                allowed = allowed & (col <= lax.broadcasted_iota(jnp.int32, (rows, rows), 0))
            bias_sc[distance] = jnp.where(allowed, jnp.float32(0.0), -jnp.inf)

    for distance in range(REACH + 1):
        rope_ref = rope_refs[distance]
        key_ref = key_refs[distance]
        value_ref = value_refs[distance]

        @pl.when(flag_ref[distance] == 0)
        def _():
            o_sc[distance] = jnp.zeros((rows, DV), jnp.float32)
            m_sc[distance] = jnp.full((rows, 1), -1e30, jnp.float32)
            l_sc[distance] = jnp.zeros((rows, 1), jnp.float32)

        @pl.when(flag_ref[distance] != 0)
        def _():
            scores = jnp.dot(qn_ref[0], key_ref[...], preferred_element_type=jnp.float32)
            scores = scores + jnp.dot(qr_ref[0], rope_ref[...], preferred_element_type=jnp.float32)
            masked = scores * score_scale + bias_sc[distance]
            block_max = jnp.maximum(jnp.max(masked, axis=1, keepdims=True), jnp.float32(-1e30))
            weights = jnp.exp(masked - block_max)
            l_sc[distance] = jnp.sum(weights, axis=1, keepdims=True)
            m_sc[distance] = block_max
            o_sc[distance] = jnp.dot(
                weights.astype(jnp.bfloat16), value_ref[...], preferred_element_type=jnp.float32
            )

    top_max = m_sc[0]
    for distance in range(1, REACH + 1):
        top_max = jnp.maximum(top_max, m_sc[distance])
    numerator = jnp.zeros((rows, DV), jnp.float32)
    denominator = jnp.zeros((rows, 1), jnp.float32)
    for distance in range(REACH + 1):
        factor = jnp.exp(m_sc[distance] - top_max)
        numerator = numerator + factor * o_sc[distance]
        denominator = denominator + factor * l_sc[distance]
    out_ref[...] = (numerator / denominator).astype(out_ref.dtype)


def attend(flags, query_nope, query_rope, rel_start, rope_blocks, key_blocks, value_blocks):
    head_count, rows, _ = query_nope.shape
    blocks = len(rope_blocks)
    flops = head_count * blocks * rows * 2 * rows * (DN + DR + DV)
    rope_spec = pl.BlockSpec((DR, rows), lambda h, f: (0, 0))
    key_spec = pl.BlockSpec((DN, rows), lambda h, f: (h, 0))
    value_spec = pl.BlockSpec((rows, DV), lambda h, f: (0, h))
    return pl.pallas_call(
        attend_kernel,
        out_shape=jax.ShapeDtypeStruct((rows, head_count * DV), jnp.bfloat16),
        grid_spec=pltpu.PrefetchScalarGridSpec(
            num_scalar_prefetch=1,
            grid=(head_count,),
            in_specs=[
                pl.BlockSpec((1, rows, DN), lambda h, f: (h, 0, 0)),
                pl.BlockSpec((1, rows, DR), lambda h, f: (h, 0, 0)),
                pl.BlockSpec((rows, 1), lambda h, f: (0, 0)),
            ]
            + [rope_spec] * blocks
            + [key_spec] * blocks
            + [value_spec] * blocks,
            out_specs=pl.BlockSpec((rows, DV), lambda h, f: (0, h)),
            scratch_shapes=[
                pltpu.VMEM((blocks, rows, DV), jnp.float32),
                pltpu.VMEM((blocks, rows, 1), jnp.float32),
                pltpu.VMEM((blocks, rows, 1), jnp.float32),
                pltpu.VMEM((blocks, rows, rows), jnp.float32),
            ],
        ),
        compiler_params=pltpu.CompilerParams(dimension_semantics=("arbitrary",)),
        cost_estimate=pl.CostEstimate(
            flops=flops, transcendentals=head_count * blocks * rows * rows, bytes_accessed=16 * 1024 * 1024
        ),
    )(flags, query_nope, query_rope, rel_start, *rope_blocks, *key_blocks, *value_blocks)


def local(queries, latent_rope, doc_start, w_kv_up, w_out):
    row_count = queries.shape[0]
    head_count = w_out.shape[0] // DV
    query_all = queries.reshape(row_count, head_count, DN + DR).transpose(1, 0, 2)
    query_nope = query_all[:, :, :DN]
    query_rope = query_all[:, :, DN:]
    device_slot = lax.axis_index("srv")
    block_first = device_slot * row_count
    rel_start = (doc_start - block_first).reshape(row_count, 1)
    lowest_start = jnp.min(doc_start)
    evens = even_distance_blocks(latent_rope)
    held_at = {2 * j: evens[j] for j in range(5)}
    for j in range(1, 5):
        held_at[2 * j - 1] = odd_distance_block(evens[j - 1], evens[j])
    distances = jnp.arange(REACH + 1, dtype=jnp.int32)
    key_last = block_first - distances * row_count + row_count - 1
    flags = (key_last >= lowest_start).astype(jnp.int32)
    latent_blocks = [held_at[d] for d in range(REACH + 1)]
    w_split = w_kv_up.reshape(R, head_count, 2, DN)
    w_key = w_split[:, :, 0, :].reshape(R, head_count * DN)
    w_value = w_split[:, :, 1, :].reshape(R, head_count * DV)
    w_key, w_value = lax.optimization_barrier((w_key, w_value))
    key_blocks = [
        jnp.einsum("jr,rc->cj", block[:, :R], w_key, preferred_element_type=jnp.float32).astype(jnp.bfloat16)
        for block in latent_blocks
    ]
    value_blocks = [
        jnp.dot(block[:, :R], w_value, preferred_element_type=jnp.float32).astype(jnp.bfloat16)
        for block in latent_blocks
    ]
    rope_blocks = [block[:, R:].T for block in latent_blocks]
    attended = attend(flags, query_nope, query_rope, rel_start, rope_blocks, key_blocks, value_blocks)
    return jnp.dot(attended, w_out, preferred_element_type=jnp.float32).astype(jnp.bfloat16)


def solution(mesh):
    in_specs = (P(("grp", "srv"), None), P(("grp", "srv"), None), P(("grp", "srv")), P(), P())
    out_specs = P(("grp", "srv"), None)
    return jax.shard_map(local, mesh=mesh, in_specs=in_specs, out_specs=out_specs, check_vma=False)
```

```python
import functools
import math

import jax
import jax.numpy as jnp
from jax import lax
from jax.experimental import pallas as pl
from jax.experimental.pallas import tpu as pltpu
from jax.sharding import PartitionSpec as P

DN = 128
DR = 64
DV = 128
R = 512
REACH = 7
EARLY = (0, 2, 4)


def moved(value, pairs):
    return lax.ppermute(value, "srv", pairs)


def even_distance_blocks(own):
    count = lax.axis_size("srv")
    slots = range(count)
    k_of = lambda s: s % 4
    near = moved(own, [(s, s + 2) for s in slots if k_of(s) < 2])
    back4 = moved(own, [(s, s + 4) for s in slots if s + 4 < count])
    across = moved(back4, [(s, s ^ 2) for s in slots])
    back8 = moved(back4, [(s, s + 4) for s in slots if s + 4 < count and k_of(s) != 0])
    far = moved(back8, [(s, s - 2) for s in slots if k_of(s) >= 2])
    low_half = lax.axis_index("srv") % 4 < 2
    dist2 = jnp.where(low_half, across, near)
    dist6 = jnp.where(low_half, far, across)
    return [own, dist2, back4, dist6, back8]


def odd_distance_block(nearer, farther):
    count = lax.axis_size("srv")
    upper_core = lax.axis_index("srv") % 2 == 1
    sent = jnp.where(upper_core, farther, nearer)
    return moved(sent, [(s, s ^ 1) for s in range(count)])


def attend_kernel(distances, carry, flag_ref, qn_ref, qr_ref, rel_ref, *rest):
    blocks = len(distances)
    rope_refs = rest[:blocks]
    key_refs = rest[blocks : 2 * blocks]
    value_refs = rest[2 * blocks : 3 * blocks]
    rest = rest[3 * blocks :]
    if carry:
        num_in_ref, stat_in_ref = rest[:2]
        rest = rest[2:]
    outs = rest[: 1 if carry else 2]
    o_sc, m_sc, l_sc, bias_sc = rest[len(outs) :]
    rows = value_refs[0].shape[0]
    score_scale = 1.0 / math.sqrt(DN + DR)

    @pl.when(pl.program_id(0) == 0)
    def _():
        col = lax.broadcasted_iota(jnp.int32, (rows, rows), 1)
        rel = rel_ref[...]
        for slot, distance in enumerate(distances):
            allowed = col >= rel + distance * rows
            if distance == 0:
                allowed = allowed & (col <= lax.broadcasted_iota(jnp.int32, (rows, rows), 0))
            bias_sc[slot] = jnp.where(allowed, jnp.float32(0.0), -jnp.inf)

    for slot in range(blocks):
        rope_ref = rope_refs[slot]
        key_ref = key_refs[slot]
        value_ref = value_refs[slot]

        @pl.when(flag_ref[slot] == 0)
        def _():
            o_sc[slot] = jnp.zeros((rows, DV), jnp.float32)
            m_sc[slot] = jnp.full((rows, 1), -1e30, jnp.float32)
            l_sc[slot] = jnp.zeros((rows, 1), jnp.float32)

        @pl.when(flag_ref[slot] != 0)
        def _():
            scores = jnp.dot(qn_ref[0], key_ref[...], preferred_element_type=jnp.float32)
            scores = scores + jnp.dot(qr_ref[0], rope_ref[...], preferred_element_type=jnp.float32)
            masked = scores * score_scale + bias_sc[slot]
            block_max = jnp.maximum(jnp.max(masked, axis=1, keepdims=True), jnp.float32(-1e30))
            weights = jnp.exp(masked - block_max)
            l_sc[slot] = jnp.sum(weights, axis=1, keepdims=True)
            m_sc[slot] = block_max
            o_sc[slot] = jnp.dot(weights.astype(jnp.bfloat16), value_ref[...], preferred_element_type=jnp.float32)

    top_max = m_sc[0]
    for slot in range(1, blocks):
        top_max = jnp.maximum(top_max, m_sc[slot])
    if carry:
        stat_in = stat_in_ref[...]
        carried_max = stat_in[:, 0:1]
        top_max = jnp.maximum(top_max, carried_max)
        carried = jnp.exp(carried_max - top_max)
        numerator = carried * num_in_ref[...]
        denominator = carried * stat_in[:, DV // 2 : DV // 2 + 1]
    else:
        numerator = jnp.zeros((rows, DV), jnp.float32)
        denominator = jnp.zeros((rows, 1), jnp.float32)
    for slot in range(blocks):
        factor = jnp.exp(m_sc[slot] - top_max)
        numerator = numerator + factor * o_sc[slot]
        denominator = denominator + factor * l_sc[slot]
    if carry:
        outs[0][...] = (numerator / denominator).astype(outs[0].dtype)
    else:
        lane = lax.broadcasted_iota(jnp.int32, (rows, DV), 1)
        outs[0][...] = numerator
        outs[1][...] = jnp.where(lane < DV // 2, top_max, denominator)


def attend(distances, flags, query_nope, query_rope, rel_start, rope_blocks, key_blocks, value_blocks, state=None):
    head_count, rows, _ = query_nope.shape
    blocks = len(distances)
    carry = state is not None
    flops = head_count * blocks * rows * 2 * rows * (DN + DR + DV)
    rope_spec = pl.BlockSpec((DR, rows), lambda h, f: (0, 0))
    key_spec = pl.BlockSpec((DN, rows), lambda h, f: (h, 0))
    head_spec = pl.BlockSpec((rows, DV), lambda h, f: (0, h))
    in_specs = [
        pl.BlockSpec((1, rows, DN), lambda h, f: (h, 0, 0)),
        pl.BlockSpec((1, rows, DR), lambda h, f: (h, 0, 0)),
        pl.BlockSpec((rows, 1), lambda h, f: (0, 0)),
    ] + [rope_spec] * blocks + [key_spec] * blocks + [head_spec] * blocks
    operands = [flags, query_nope, query_rope, rel_start, *rope_blocks, *key_blocks, *value_blocks]
    if carry:
        in_specs += [head_spec, head_spec]
        operands += list(state)
        out_shape = jax.ShapeDtypeStruct((rows, head_count * DV), jnp.bfloat16)
        out_specs = head_spec
    else:
        out_shape = (
            jax.ShapeDtypeStruct((rows, head_count * DV), jnp.float32),
            jax.ShapeDtypeStruct((rows, head_count * DV), jnp.float32),
        )
        out_specs = [head_spec, head_spec]
    return pl.pallas_call(
        functools.partial(attend_kernel, tuple(distances), carry),
        out_shape=out_shape,
        grid_spec=pltpu.PrefetchScalarGridSpec(
            num_scalar_prefetch=1,
            grid=(head_count,),
            in_specs=in_specs,
            out_specs=out_specs,
            scratch_shapes=[
                pltpu.VMEM((blocks, rows, DV), jnp.float32),
                pltpu.VMEM((blocks, rows, 1), jnp.float32),
                pltpu.VMEM((blocks, rows, 1), jnp.float32),
                pltpu.VMEM((blocks, rows, rows), jnp.float32),
            ],
        ),
        compiler_params=pltpu.CompilerParams(dimension_semantics=("arbitrary",)),
        cost_estimate=pl.CostEstimate(
            flops=flops, transcendentals=head_count * blocks * rows * rows, bytes_accessed=2 * blocks * 1024 * 1024
        ),
    )(*operands)


def local(queries, latent_rope, doc_start, w_kv_up, w_out):
    row_count = queries.shape[0]
    head_count = w_out.shape[0] // DV
    query_all = queries.reshape(row_count, head_count, DN + DR).transpose(1, 0, 2)
    query_nope = query_all[:, :, :DN]
    query_rope = query_all[:, :, DN:]
    device_slot = lax.axis_index("srv")
    block_first = device_slot * row_count
    rel_start = (doc_start - block_first).reshape(row_count, 1)
    lowest_start = jnp.min(doc_start)
    evens = even_distance_blocks(latent_rope)
    held_at = {2 * j: evens[j] for j in range(5)}
    for j in range(1, 5):
        held_at[2 * j - 1] = odd_distance_block(evens[j - 1], evens[j])
    distances = jnp.arange(REACH + 1, dtype=jnp.int32)
    key_last = block_first - distances * row_count + row_count - 1
    flags = (key_last >= lowest_start).astype(jnp.int32)
    latent_blocks = [held_at[d] for d in range(REACH + 1)]
    w_split = w_kv_up.reshape(R, head_count, 2, DN)
    w_key = w_split[:, :, 0, :].reshape(R, head_count * DN)
    w_value = w_split[:, :, 1, :].reshape(R, head_count * DV)
    w_key, w_value = lax.optimization_barrier((w_key, w_value))
    key_blocks = [
        jnp.einsum("jr,rc->cj", block[:, :R], w_key, preferred_element_type=jnp.float32).astype(jnp.bfloat16)
        for block in latent_blocks
    ]
    value_blocks = [
        jnp.dot(block[:, :R], w_value, preferred_element_type=jnp.float32).astype(jnp.bfloat16)
        for block in latent_blocks
    ]
    rope_blocks = [block[:, R:].T for block in latent_blocks]

    def group(chosen, state=None):
        return attend(
            chosen,
            flags[jnp.array(chosen)],
            query_nope,
            query_rope,
            rel_start,
            [rope_blocks[d] for d in chosen],
            [key_blocks[d] for d in chosen],
            [value_blocks[d] for d in chosen],
            state,
        )

    early = group(EARLY)
    attended = group(tuple(d for d in range(REACH + 1) if d not in EARLY), early)
    return jnp.dot(attended, w_out, preferred_element_type=jnp.float32).astype(jnp.bfloat16)


def solution(mesh):
    in_specs = (P(("grp", "srv"), None), P(("grp", "srv"), None), P(("grp", "srv")), P(), P())
    out_specs = P(("grp", "srv"), None)
    return jax.shard_map(local, mesh=mesh, in_specs=in_specs, out_specs=out_specs, check_vma=False)
```

```python
import math

import jax
import jax.numpy as jnp
from jax import lax
from jax.sharding import PartitionSpec as P

DN = 128
DR = 64
DV = 128
R = 512
REACH = 7


def moved(value, pairs):
    return lax.ppermute(value, "srv", pairs)


def even_distance_blocks(own):
    count = lax.axis_size("srv")
    slots = range(count)
    k_of = lambda s: s % 4
    near = moved(own, [(s, s + 2) for s in slots if k_of(s) < 2])
    back4 = moved(own, [(s, s + 4) for s in slots if s + 4 < count])
    across = moved(back4, [(s, s ^ 2) for s in slots])
    back8 = moved(back4, [(s, s + 4) for s in slots if s + 4 < count and k_of(s) != 0])
    far = moved(back8, [(s, s - 2) for s in slots if k_of(s) >= 2])
    low_half = lax.axis_index("srv") % 4 < 2
    dist2 = jnp.where(low_half, across, near)
    dist6 = jnp.where(low_half, far, across)
    return [own, dist2, back4, dist6, back8]


def odd_distance_block(nearer, farther):
    count = lax.axis_size("srv")
    upper_core = lax.axis_index("srv") % 2 == 1
    sent = jnp.where(upper_core, farther, nearer)
    return moved(sent, [(s, s ^ 1) for s in range(count)])


def expand_rows(latent_part, w_kv_up, head_count):
    row_count = latent_part.shape[0]
    product = jnp.dot(latent_part, w_kv_up, preferred_element_type=jnp.float32)
    return product.astype(jnp.bfloat16).reshape(row_count, head_count, -1)


def block_terms(query_nope, query_rope, key_nope, values, key_rope, query_pos, key_pos, starts):
    score_scale = 1.0 / math.sqrt(query_nope.shape[-1] + query_rope.shape[-1])
    scores = jnp.einsum("ihc,jhc->hij", query_nope, key_nope, preferred_element_type=jnp.float32)
    scores = scores + jnp.einsum(
        "ihc,jc->hij", query_rope, key_rope, preferred_element_type=jnp.float32
    )
    scores = scores * score_scale
    allowed = (key_pos[None, :] >= starts[:, None]) & (key_pos[None, :] <= query_pos[:, None])
    bias = jnp.where(allowed, jnp.float32(0.0), -jnp.inf)
    masked = scores + bias[None]
    block_max = jnp.maximum(jnp.max(masked, axis=2), jnp.float32(-1e30))
    weights = jnp.exp(masked - block_max[:, :, None])
    block_total = jnp.sum(weights, axis=2)
    block_out = jnp.einsum(
        "hij,jhc->ihc", weights.astype(jnp.bfloat16), values, preferred_element_type=jnp.float32
    )
    return (block_out, block_max, block_total)


def merge_blocks(pieces):
    top_max = pieces[0][1]
    for block_part in pieces[1:]:
        top_max = jnp.maximum(top_max, block_part[1])
    numerator = jnp.zeros(pieces[0][0].shape, jnp.float32)
    denominator = jnp.zeros(pieces[0][0].shape[:2] + (1,), jnp.float32)
    for block_part in pieces:
        factor = jnp.exp(block_part[1] - top_max)
        numerator = numerator + factor.T[:, :, None] * block_part[0]
        denominator = denominator + (factor * block_part[2]).T[:, :, None]
    return (numerator / denominator).astype(jnp.bfloat16)


def local(queries, latent_rope, doc_start, w_kv_up, w_out):
    row_count = queries.shape[0]
    head_count = w_out.shape[0] // DV
    query_all = queries.reshape(row_count, head_count, DN + DR)
    query_nope = query_all[:, :, :DN]
    query_rope = query_all[:, :, DN:]
    device_slot = lax.axis_index("srv")
    query_pos = device_slot * row_count + jnp.arange(row_count, dtype=jnp.int32)
    evens = even_distance_blocks(latent_rope)
    held_at = {2 * j: evens[j] for j in range(5)}
    for j in range(1, 5):
        held_at[2 * j - 1] = odd_distance_block(evens[j - 1], evens[j])
    pieces = []
    for distance in range(REACH + 1):
        held = held_at[distance]
        key_kv = expand_rows(held[:, :R], w_kv_up, head_count)
        key_rope = held[:, R:]
        key_pos = query_pos - distance * row_count
        pieces.append(
            block_terms(
                query_nope,
                query_rope,
                key_kv[:, :, :DN],
                key_kv[:, :, DN:],
                key_rope,
                query_pos,
                key_pos,
                doc_start,
            )
        )
    attended = merge_blocks(pieces).reshape(row_count, head_count * DV)
    return jnp.dot(attended, w_out, preferred_element_type=jnp.float32).astype(jnp.bfloat16)


def solution(mesh):
    in_specs = (P(("grp", "srv"), None), P(("grp", "srv"), None), P(("grp", "srv")), P(), P())
    out_specs = P(("grp", "srv"), None)
    return jax.shard_map(local, mesh=mesh, in_specs=in_specs, out_specs=out_specs, check_vma=False)
```

```python
import math

import jax
import jax.numpy as jnp
from jax import lax
from jax.sharding import PartitionSpec as P

DN = 128
DR = 64
DV = 128
R = 512
REACH = 7


def moved(value, pairs):
    return lax.ppermute(value, "srv", pairs)


def even_distance_blocks(own):
    count = lax.axis_size("srv")
    slots = range(count)
    k_of = lambda s: s % 4
    near = moved(own, [(s, s + 2) for s in slots if k_of(s) < 2])
    back4 = moved(own, [(s, s + 4) for s in slots if s + 4 < count])
    across = moved(back4, [(s, s ^ 2) for s in slots])
    back8 = moved(back4, [(s, s + 4) for s in slots if s + 4 < count and k_of(s) != 0])
    far = moved(back8, [(s, s - 2) for s in slots if k_of(s) >= 2])
    low_half = lax.axis_index("srv") % 4 < 2
    dist2 = jnp.where(low_half, across, near)
    dist6 = jnp.where(low_half, far, across)
    return [own, dist2, back4, dist6, back8]


def odd_distance_block(nearer, farther):
    count = lax.axis_size("srv")
    upper_core = lax.axis_index("srv") % 2 == 1
    sent = jnp.where(upper_core, farther, nearer)
    return moved(sent, [(s, s ^ 1) for s in range(count)])


def expand_rows(latent_part, w_kv_up, head_count):
    row_count = latent_part.shape[0]
    product = jnp.dot(latent_part, w_kv_up, preferred_element_type=jnp.float32)
    return product.astype(jnp.bfloat16).reshape(row_count, head_count, -1)


def block_terms(query_nope, query_rope, key_nope, values, key_rope, query_pos, key_pos, starts, causal):
    score_scale = 1.0 / math.sqrt(query_nope.shape[-1] + query_rope.shape[-1])
    scores = jnp.einsum("ihc,jhc->hij", query_nope, key_nope, preferred_element_type=jnp.float32)
    scores = scores + jnp.einsum(
        "ihc,jc->hij", query_rope, key_rope, preferred_element_type=jnp.float32
    )
    scores = scores * score_scale
    allowed = key_pos[None, :] >= starts[:, None]
    if causal:
        allowed = allowed & (key_pos[None, :] <= query_pos[:, None])
    bias = jnp.where(allowed, jnp.float32(0.0), -jnp.inf)
    masked = scores + bias[None]
    block_max = jnp.maximum(jnp.max(masked, axis=2), jnp.float32(-1e30))
    weights = jnp.exp(masked - block_max[:, :, None])
    block_total = jnp.sum(weights, axis=2)
    block_out = jnp.einsum(
        "hij,jhc->ihc", weights.astype(jnp.bfloat16), values, preferred_element_type=jnp.float32
    )
    return (block_out, block_max, block_total)


def merge_blocks(pieces):
    top_max = pieces[0][1]
    for block_part in pieces[1:]:
        top_max = jnp.maximum(top_max, block_part[1])
    numerator = jnp.zeros(pieces[0][0].shape, jnp.float32)
    denominator = jnp.zeros(pieces[0][0].shape[:2] + (1,), jnp.float32)
    for block_part in pieces:
        factor = jnp.exp(block_part[1] - top_max)
        numerator = numerator + factor.T[:, :, None] * block_part[0]
        denominator = denominator + (factor * block_part[2]).T[:, :, None]
    return (numerator / denominator).astype(jnp.bfloat16)


def local(queries, latent_rope, doc_start, w_kv_up, w_out):
    row_count = queries.shape[0]
    head_count = w_out.shape[0] // DV
    query_all = queries.reshape(row_count, head_count, DN + DR)
    query_nope = query_all[:, :, :DN]
    query_rope = query_all[:, :, DN:]
    device_slot = lax.axis_index("srv")
    query_pos = device_slot * row_count + jnp.arange(row_count, dtype=jnp.int32)
    evens = even_distance_blocks(latent_rope)
    held_at = {2 * j: evens[j] for j in range(5)}
    for j in range(1, 5):
        held_at[2 * j - 1] = odd_distance_block(evens[j - 1], evens[j])
    pieces = []
    for distance in range(REACH + 1):
        held = held_at[distance]
        key_kv = expand_rows(held[:, :R], w_kv_up, head_count)
        key_rope = held[:, R:]
        key_pos = query_pos - distance * row_count
        pieces.append(
            block_terms(
                query_nope,
                query_rope,
                key_kv[:, :, :DN],
                key_kv[:, :, DN:],
                key_rope,
                query_pos,
                key_pos,
                doc_start,
                distance == 0,
            )
        )
    attended = merge_blocks(pieces).reshape(row_count, head_count * DV)
    return jnp.dot(attended, w_out, preferred_element_type=jnp.float32).astype(jnp.bfloat16)


def solution(mesh):
    in_specs = (P(("grp", "srv"), None), P(("grp", "srv"), None), P(("grp", "srv")), P(), P())
    out_specs = P(("grp", "srv"), None)
    return jax.shard_map(local, mesh=mesh, in_specs=in_specs, out_specs=out_specs, check_vma=False)
```

```python
import math

import jax
import jax.numpy as jnp
from jax import lax
from jax.sharding import PartitionSpec as P

DN = 128
DR = 64
DV = 128
R = 512
REACH = 7


def moved(value, pairs):
    return lax.ppermute(value, "srv", pairs)


def even_distance_blocks(own):
    count = lax.axis_size("srv")
    slots = range(count)
    k_of = lambda s: s % 4
    near = moved(own, [(s, s + 2) for s in slots if k_of(s) < 2])
    back4 = moved(own, [(s, s + 4) for s in slots if s + 4 < count])
    across = moved(back4, [(s, s ^ 2) for s in slots])
    back8 = moved(back4, [(s, s + 4) for s in slots if s + 4 < count and k_of(s) != 0])
    far = moved(back8, [(s, s - 2) for s in slots if k_of(s) >= 2])
    low_half = lax.axis_index("srv") % 4 < 2
    dist2 = jnp.where(low_half, across, near)
    dist6 = jnp.where(low_half, far, across)
    return [own, dist2, back4, dist6, back8]


def odd_distance_block(nearer, farther):
    count = lax.axis_size("srv")
    upper_core = lax.axis_index("srv") % 2 == 1
    sent = jnp.where(upper_core, farther, nearer)
    return moved(sent, [(s, s ^ 1) for s in range(count)])


def expand_rows(latent_part, weights, head_count):
    product = jnp.einsum("jr,rhc->hjc", latent_part, weights, preferred_element_type=jnp.float32)
    return product.astype(jnp.bfloat16)


def block_terms(query_nope, query_rope, key_nope, values, key_rope, query_pos, key_pos, starts, causal):
    score_scale = 1.0 / math.sqrt(query_nope.shape[-1] + query_rope.shape[-1])
    scores = jnp.einsum("ihc,hjc->hij", query_nope, key_nope, preferred_element_type=jnp.float32)
    scores = scores + jnp.einsum(
        "ihc,jc->hij", query_rope, key_rope, preferred_element_type=jnp.float32
    )
    scores = scores * score_scale
    allowed = key_pos[None, :] >= starts[:, None]
    if causal:
        allowed = allowed & (key_pos[None, :] <= query_pos[:, None])
    bias = jnp.where(allowed, jnp.float32(0.0), -jnp.inf)
    masked = scores + bias[None]
    block_max = jnp.maximum(jnp.max(masked, axis=2), jnp.float32(-1e30))
    weights = jnp.exp(masked - block_max[:, :, None])
    block_total = jnp.sum(weights, axis=2)
    block_out = jnp.einsum(
        "hij,hjc->ihc", weights.astype(jnp.bfloat16), values, preferred_element_type=jnp.float32
    )
    return (block_out, block_max, block_total)


def merge_blocks(pieces):
    top_max = pieces[0][1]
    for block_part in pieces[1:]:
        top_max = jnp.maximum(top_max, block_part[1])
    numerator = jnp.zeros(pieces[0][0].shape, jnp.float32)
    denominator = jnp.zeros(pieces[0][0].shape[:2] + (1,), jnp.float32)
    for block_part in pieces:
        factor = jnp.exp(block_part[1] - top_max)
        numerator = numerator + factor.T[:, :, None] * block_part[0]
        denominator = denominator + (factor * block_part[2]).T[:, :, None]
    return (numerator / denominator).astype(jnp.bfloat16)


def local(queries, latent_rope, doc_start, w_kv_up, w_out):
    row_count = queries.shape[0]
    head_count = w_out.shape[0] // DV
    query_all = queries.reshape(row_count, head_count, DN + DR)
    query_nope = query_all[:, :, :DN]
    query_rope = query_all[:, :, DN:]
    device_slot = lax.axis_index("srv")
    query_pos = device_slot * row_count + jnp.arange(row_count, dtype=jnp.int32)
    head_weights = lax.optimization_barrier(w_kv_up.reshape(R, head_count, DN + DV))
    evens = even_distance_blocks(latent_rope)
    held_at = {2 * j: evens[j] for j in range(5)}
    for j in range(1, 5):
        held_at[2 * j - 1] = odd_distance_block(evens[j - 1], evens[j])
    pieces = []
    for distance in range(REACH + 1):
        held = held_at[distance]
        key_kv = expand_rows(held[:, :R], head_weights, head_count)
        key_rope = held[:, R:]
        key_pos = query_pos - distance * row_count
        pieces.append(
            block_terms(
                query_nope,
                query_rope,
                key_kv[:, :, :DN],
                key_kv[:, :, DN:],
                key_rope,
                query_pos,
                key_pos,
                doc_start,
                distance == 0,
            )
        )
    attended = merge_blocks(pieces).reshape(row_count, head_count * DV)
    return jnp.dot(attended, w_out, preferred_element_type=jnp.float32).astype(jnp.bfloat16)


def solution(mesh):
    in_specs = (P(("grp", "srv"), None), P(("grp", "srv"), None), P(("grp", "srv")), P(), P())
    out_specs = P(("grp", "srv"), None)
    return jax.shard_map(local, mesh=mesh, in_specs=in_specs, out_specs=out_specs, check_vma=False)
```

```python
import math

import jax
import jax.numpy as jnp
from jax import lax
from jax.sharding import PartitionSpec as P

DN = 128
DR = 64
DV = 128
R = 512
REACH = 7


def moved(value, pairs):
    return lax.ppermute(value, "srv", pairs)


def even_distance_blocks(own):
    count = lax.axis_size("srv")
    slots = range(count)
    k_of = lambda s: s % 4
    near = moved(own, [(s, s + 2) for s in slots if k_of(s) < 2])
    back4 = moved(own, [(s, s + 4) for s in slots if s + 4 < count])
    across = moved(back4, [(s, s ^ 2) for s in slots])
    back8 = moved(back4, [(s, s + 4) for s in slots if s + 4 < count and k_of(s) != 0])
    far = moved(back8, [(s, s - 2) for s in slots if k_of(s) >= 2])
    low_half = lax.axis_index("srv") % 4 < 2
    dist2 = jnp.where(low_half, across, near)
    dist6 = jnp.where(low_half, far, across)
    return [own, dist2, back4, dist6, back8]


def odd_distance_block(nearer, farther):
    count = lax.axis_size("srv")
    upper_core = lax.axis_index("srv") % 2 == 1
    sent = jnp.where(upper_core, farther, nearer)
    return moved(sent, [(s, s ^ 1) for s in range(count)])


def expand_rows(latent_part, weights, head_count):
    product = jnp.einsum("jr,hrc->hjc", latent_part, weights, preferred_element_type=jnp.float32)
    return product.astype(jnp.bfloat16)


def block_terms(query_nope, query_rope, key_nope, values, key_rope, query_pos, key_pos, starts, causal):
    score_scale = 1.0 / math.sqrt(query_nope.shape[-1] + query_rope.shape[-1])
    scores = jnp.einsum("ihc,hjc->hij", query_nope, key_nope, preferred_element_type=jnp.float32)
    scores = scores + jnp.einsum(
        "ihc,jc->hij", query_rope, key_rope, preferred_element_type=jnp.float32
    )
    scores = scores * score_scale
    allowed = key_pos[None, :] >= starts[:, None]
    if causal:
        allowed = allowed & (key_pos[None, :] <= query_pos[:, None])
    bias = jnp.where(allowed, jnp.float32(0.0), -jnp.inf)
    masked = scores + bias[None]
    block_max = jnp.maximum(jnp.max(masked, axis=2), jnp.float32(-1e30))
    weights = jnp.exp(masked - block_max[:, :, None])
    block_total = jnp.sum(weights, axis=2)
    block_out = jnp.einsum(
        "hij,hjc->ihc", weights.astype(jnp.bfloat16), values, preferred_element_type=jnp.float32
    )
    return (block_out, block_max, block_total)


def merge_blocks(pieces):
    top_max = pieces[0][1]
    for block_part in pieces[1:]:
        top_max = jnp.maximum(top_max, block_part[1])
    numerator = jnp.zeros(pieces[0][0].shape, jnp.float32)
    denominator = jnp.zeros(pieces[0][0].shape[:2] + (1,), jnp.float32)
    for block_part in pieces:
        factor = jnp.exp(block_part[1] - top_max)
        numerator = numerator + factor.T[:, :, None] * block_part[0]
        denominator = denominator + (factor * block_part[2]).T[:, :, None]
    return (numerator / denominator).astype(jnp.bfloat16)


def local(queries, latent_rope, doc_start, w_kv_up, w_out):
    row_count = queries.shape[0]
    head_count = w_out.shape[0] // DV
    query_all = queries.reshape(row_count, head_count, DN + DR)
    query_nope = query_all[:, :, :DN]
    query_rope = query_all[:, :, DN:]
    device_slot = lax.axis_index("srv")
    query_pos = device_slot * row_count + jnp.arange(row_count, dtype=jnp.int32)
    head_weights = lax.optimization_barrier(w_kv_up.reshape(R, head_count, DN + DV).transpose(1, 0, 2))
    evens = even_distance_blocks(latent_rope)
    held_at = {2 * j: evens[j] for j in range(5)}
    for j in range(1, 5):
        held_at[2 * j - 1] = odd_distance_block(evens[j - 1], evens[j])
    pieces = []
    for distance in range(REACH + 1):
        held = held_at[distance]
        key_kv = expand_rows(held[:, :R], head_weights, head_count)
        key_rope = held[:, R:]
        key_pos = query_pos - distance * row_count
        pieces.append(
            block_terms(
                query_nope,
                query_rope,
                key_kv[:, :, :DN],
                key_kv[:, :, DN:],
                key_rope,
                query_pos,
                key_pos,
                doc_start,
                distance == 0,
            )
        )
    attended = merge_blocks(pieces).reshape(row_count, head_count * DV)
    return jnp.dot(attended, w_out, preferred_element_type=jnp.float32).astype(jnp.bfloat16)


def solution(mesh):
    in_specs = (P(("grp", "srv"), None), P(("grp", "srv"), None), P(("grp", "srv")), P(), P())
    out_specs = P(("grp", "srv"), None)
    return jax.shard_map(local, mesh=mesh, in_specs=in_specs, out_specs=out_specs, check_vma=False)
```
